1024 devices in a mesh: row: 32 (over x, y, z_hi), col: 32 (over z_lo, core).
Axes of the slice: x: 4, y: 4, z: 32 (z_hi: 2, z_lo: 16; z = z_hi * 16 + z_lo), core: 2. Of those that a mesh axis runs over, the one named last changes fastest.
Arguments:
- density: float32 [1024, 7, 128, 128], P(('row', 'col')), as said below
- pattern: int32 [1024, 12], P(('row', 'col')), may hold values from 0 to 1023, as said below
Outputs:
- purified: float32 [1024, 7, 128, 128], P(('row', 'col'))
The draws below stay inside these ranges and needn't reach their ends.
Inputs may be any that keep to these rules, and one draw needn't show every extreme that they name: `pattern`: row I lists the block columns (I + o) mod 1024 for o = -6..6 in rising order of o, all but one o; the omitted o is nonzero and of magnitude 3 or less, and row (I + o) mod 1024 omits -o. density[I, 0] is symmetric, and density[I, t] is zero where (I + t) mod 1024 is not listed in row I of pattern.
All inputs are finite; a program needn't handle non-finite values.
Results may differ from the reference program's by a relative error of at most 0.0001.
Values sent between devices are 32-bit elements; how exact they have to be, the bound alone decides.
No kernel may reach another device: no remote copies, remote signals or barrier semaphores. Data moves between devices by JAX's collectives and lax.ppermute only.
A program may use at most 32 MiB of HBM per device.

```python
import jax
import jax.numpy as jnp
from jax import lax

BLOCK = 128
REACH = 6
PER_ROW = 12
BLOCKS = 1024


def partner_offsets(key):
    picks = jax.random.randint(jax.random.fold_in(key, 11), (BLOCKS // 4,), 0, 3)
    table = jnp.array([[1, -1, 1, -1], [2, 2, -2, -2], [3, 1, -1, -3]], jnp.int32)
    return table[picks].reshape(BLOCKS).astype(jnp.int32)


def draw_pattern(key, part):
    partner = partner_offsets(key)
    removed = partner + REACH
    kept = jnp.arange(PER_ROW, dtype=jnp.int32)[None, :]
    index = kept + (kept >= removed[:, None]).astype(jnp.int32)
    offsets = index - REACH
    listed = jnp.arange(BLOCKS, dtype=jnp.int32)[:, None]
    return ((listed + offsets + BLOCKS) % BLOCKS).astype(jnp.int32)


def draw_density(key, part):
    partner = partner_offsets(key)
    value_key = jax.random.fold_in(key, 23)
    shape = (BLOCKS, REACH + 1, BLOCK, BLOCK)
    spread = 1.5 / (PER_ROW * BLOCK) ** 0.5
    raw = jax.random.normal(value_key, shape, jnp.float32)
    diagonal = (raw[:, 0] + jnp.swapaxes(raw[:, 0], 1, 2)) * 0.5
    beside = raw[:, 1:] * 0.70710678
    band = jnp.concatenate([diagonal[:, None], beside], axis=1)
    keep = (jnp.arange(REACH + 1, dtype=jnp.int32)[None, :] != partner[:, None]).astype(jnp.float32)
    return (band * spread * keep[:, :, None, None]).astype(jnp.float32)


def setup_inputs(seed: int = 0) -> dict:
    arg_keys = jax.random.split(jax.random.key(seed), 3)
    density = draw_density(jax.random.fold_in(arg_keys[2], 71), 0)
    pattern = draw_pattern(jax.random.fold_in(arg_keys[2], 71), 0)
    return dict(density=density, pattern=pattern)


def upper_block(band, offset, width):
    return jnp.roll(band[:, width], -offset, axis=0)


def block_at(band, inner, target):
    if target >= inner:
        return upper_block(band, inner, target - inner)
    return jnp.swapaxes(upper_block(band, target, inner - target), 1, 2)


def band_product(band_left, band_right):
    results = []
    for target in range(REACH + 1):
        total = jnp.zeros((BLOCKS, BLOCK, BLOCK), jnp.float32)
        for inner in range(target - REACH, REACH + 1):
            left = block_at(band_left, 0, inner).astype(jnp.float32)
            right = block_at(band_right, inner, target).astype(jnp.float32)
            total = total + jnp.einsum("zab,zbc->zac", left, right, precision=lax.Precision.HIGHEST, preferred_element_type=jnp.float32)
        results.append(total)
    return jnp.stack(results, axis=1)


def reference(density, pattern):
    listed = jnp.arange(BLOCKS, dtype=jnp.int32)
    columns = (listed[:, None] + jnp.arange(REACH + 1, dtype=jnp.int32)[None, :]) % BLOCKS
    flags = jnp.any(pattern[:, None, :] == columns[:, :, None], axis=2).astype(jnp.float32)[:, :, None, None]
    square = flags * band_product(density, density)
    cube = flags * band_product(density, square)
    return 3.0 * square - 2.0 * cube
```

```python
import jax
import jax.numpy as jnp
from jax import lax
from jax.sharding import PartitionSpec as P

REACH = 6
WIDTH = REACH + 1
AXES = ("row", "col")
CHIPS_OUT = 3
FLOW_BASE = {1: 0, 2: 11, 3: 18}


def swap_in_chip(x, n):
    return lax.ppermute(x, AXES, [(i, i ^ 1) for i in range(n)])


def exchange(x, is_odd, n):
    partner = swap_in_chip(x, n)
    r0 = jnp.where(is_odd, partner, x)
    r1 = jnp.where(is_odd, x, partner)
    received = []
    for d in range(1, CHIPS_OUT + 1):
        up = jnp.concatenate([r1[2 * d - 1:], r0[2 * d:]], axis=0)
        down = jnp.concatenate([r0[: 8 - 2 * d], r1[: 7 - 2 * d]], axis=0)
        buf = jnp.where(is_odd, up, down)
        step = 2 * d - 1
        route = [(i, (i + step) % n) if i % 2 else (i, (i - step) % n) for i in range(n)]
        received.append(lax.ppermute(buf, AXES, route))
    got = jnp.concatenate(received, axis=0)
    other = swap_in_chip(got, n)
    from_below_chips = jnp.where(is_odd, other, got)
    from_above_chips = jnp.where(is_odd, got, other)
    return r0, r1, from_below_chips, from_above_chips


def block_source(k, o, w, r0, r1, lower, upper):
    q = k + o
    if q == 0:
        return r0[w]
    if q == 1:
        return r1[w]
    if q < 0:
        d = (-q + 1) // 2
        base = FLOW_BASE[d]
        if -q % 2 == 1:
            return lower[base + w - (2 * d - 1)]
        return lower[base + (8 - 2 * d) + w - 2 * d]
    d = q // 2
    base = FLOW_BASE[d]
    if q % 2 == 0:
        return upper[base + w]
    return upper[base + (8 - 2 * d) + w]


def band_window(x, is_odd, n):
    r0, r1, lower, upper = exchange(x, is_odd, n)

    def get(o, w):
        even = block_source(0, o, w, r0, r1, lower, upper)
        odd = block_source(1, o, w, r0, r1, lower, upper)
        return jnp.where(is_odd, odd, even)

    zero = jnp.zeros(x.shape[1:], x.dtype)
    rows = []
    for o in range(-REACH, REACH + 1):
        blocks = []
        for t in range(WIDTH):
            if abs(t - o) > REACH:
                blocks.append(zero)
            elif t >= o:
                blocks.append(get(o, t - o))
            else:
                blocks.append(get(t, o - t).T)
        rows.append(jnp.stack(blocks, axis=1))
    window = jnp.stack(rows, axis=0)
    b = x.shape[-1]
    return window.reshape((2 * REACH + 1) * b, WIDTH * b)


def row_product(left_col, window):
    b = left_col.shape[1]
    out = lax.dot_general(
        left_col,
        window,
        (((0,), (0,)), ((), ())),
        precision=lax.Precision.HIGHEST,
        preferred_element_type=jnp.float32,
    )
    return out.reshape(b, WIDTH, b).transpose(1, 0, 2)


def on_device(density, pattern):
    local_band = density[0]
    n = lax.axis_size("row") * lax.axis_size("col")
    position = lax.axis_index("row") * lax.axis_size("col") + lax.axis_index("col")
    is_odd = (position % 2) == 1
    columns = (position + jnp.arange(WIDTH, dtype=jnp.int32)) % n
    flags = jnp.any(pattern[0][None, :] == columns[:, None], axis=1).astype(jnp.float32)[
        :, None, None
    ]
    b = local_band.shape[-1]
    window_p = band_window(local_band, is_odd, n)
    left_col = window_p[:, :b]
    square = flags * row_product(left_col, window_p)
    window_q = band_window(square, is_odd, n)
    cube = flags * row_product(left_col, window_q)
    return (3.0 * square - 2.0 * cube)[None]


def solution(mesh):
    return jax.shard_map(
        on_device,
        mesh=mesh,
        in_specs=(P(AXES, None, None, None), P(AXES, None)),
        out_specs=P(AXES, None, None, None),
        check_vma=False,
    )
```

```python
import jax
import jax.numpy as jnp
from jax import lax
from jax.sharding import PartitionSpec as P

REACH = 6
WIDTH = REACH + 1
AXES = ("row", "col")
CHIPS_OUT = 3
FLOW_BASE = {1: 0, 2: 11, 3: 18}


def swap_in_chip(x, n):
    return lax.ppermute(x, AXES, [(i, i ^ 1) for i in range(n)])


def exchange(x, is_odd, n):
    partner = swap_in_chip(x, n)
    r0 = jnp.where(is_odd, partner, x)
    r1 = jnp.where(is_odd, x, partner)
    received = []
    for d in range(1, CHIPS_OUT + 1):
        up = jnp.concatenate([r1[2 * d - 1:], r0[2 * d:]], axis=0)
        down = jnp.concatenate([r0[: 8 - 2 * d], r1[: 7 - 2 * d]], axis=0)
        buf = jnp.where(is_odd, up, down)
        step = 2 * d - 1
        route = [(i, (i + step) % n) if i % 2 else (i, (i - step) % n) for i in range(n)]
        received.append(lax.ppermute(buf, AXES, route))
    got = jnp.concatenate(received, axis=0)
    other = swap_in_chip(got, n)
    from_below_chips = jnp.where(is_odd, other, got)
    from_above_chips = jnp.where(is_odd, got, other)
    return r0, r1, from_below_chips, from_above_chips


def block_source(k, o, w, r0, r1, lower, upper):
    q = k + o
    if q == 0:
        return r0[w]
    if q == 1:
        return r1[w]
    if q < 0:
        d = (-q + 1) // 2
        base = FLOW_BASE[d]
        if -q % 2 == 1:
            return lower[base + w - (2 * d - 1)]
        return lower[base + (8 - 2 * d) + w - 2 * d]
    d = q // 2
    base = FLOW_BASE[d]
    if q % 2 == 0:
        return upper[base + w]
    return upper[base + (8 - 2 * d) + w]


def fetch_rows(x, is_odd, n):
    r0, r1, lower, upper = exchange(x, is_odd, n)

    def gather(k, sign):
        blocks = []
        for d in range(1, REACH + 1):
            widths = range(d, WIDTH) if sign < 0 else range(WIDTH - d)
            blocks += [block_source(k, sign * d, w, r0, r1, lower, upper) for w in widths]
        return jnp.stack(blocks, axis=0)

    above = jnp.where(is_odd, gather(1, -1), gather(0, -1))
    below = jnp.where(is_odd, gather(1, 1), gather(0, 1))
    rows_above, rows_below = [], []
    start = 0
    for d in range(1, REACH + 1):
        rows_above.append(above[start:start + WIDTH - d])
        rows_below.append(below[start:start + WIDTH - d])
        start += WIDTH - d
    return rows_above, rows_below


def make_upper(local_band, rows_above, rows_below):

    def upper_block(offset, width):
        if offset == 0:
            return local_band[width]
        if offset < 0:
            return rows_above[-offset - 1][width + offset]
        return rows_below[offset - 1][width]

    return upper_block


def left_operand(upper_block, inner):
    if inner >= 0:
        return (upper_block(0, inner), 1)
    return (upper_block(inner, -inner), 0)


def right_operand(upper_block, inner, target):
    if target >= inner:
        return (upper_block(inner, target - inner), 0)
    return (upper_block(target, inner - target), 1)


def band_product(upper_left, upper_right):
    results = []
    for target in range(REACH + 1):
        total = None
        for inner in range(target - REACH, REACH + 1):
            left_block, left_dim = left_operand(upper_left, inner)
            right_block, right_dim = right_operand(upper_right, inner, target)
            term = lax.dot_general(
                left_block,
                right_block,
                (((left_dim,), (right_dim,)), ((), ())),
                precision=lax.Precision.HIGHEST,
                preferred_element_type=jnp.float32,
            )
            total = term if total is None else total + term
        results.append(total)
    return jnp.stack(results, axis=0)


def on_device(density, pattern):
    local_band = density[0]
    n = lax.axis_size("row") * lax.axis_size("col")
    position = lax.axis_index("row") * lax.axis_size("col") + lax.axis_index("col")
    is_odd = (position % 2) == 1
    columns = (position + jnp.arange(WIDTH, dtype=jnp.int32)) % n
    flags = jnp.any(pattern[0][None, :] == columns[:, None], axis=1).astype(jnp.float32)[
        :, None, None
    ]
    above_p, below_p = fetch_rows(local_band, is_odd, n)
    upper_p = make_upper(local_band, above_p, below_p)
    square = flags * band_product(upper_p, upper_p)
    above_s, below_s = fetch_rows(square, is_odd, n)
    upper_s = make_upper(square, above_s, below_s)
    cube = flags * band_product(upper_p, upper_s)
    return (3.0 * square - 2.0 * cube)[None]


def solution(mesh):
    return jax.shard_map(
        on_device,
        mesh=mesh,
        in_specs=(P(AXES, None, None, None), P(AXES, None)),
        out_specs=P(AXES, None, None, None),
        check_vma=False,
    )
```

```python
import jax
import jax.numpy as jnp
from jax import lax
from jax.sharding import PartitionSpec as P

REACH = 6
WIDTH = REACH + 1
AXES = ("row", "col")
CHIPS_OUT = 3
FLOW_BASE = {1: 0, 2: 11, 3: 18}


def swap_in_chip(x, n):
    return lax.ppermute(x, AXES, [(i, i ^ 1) for i in range(n)])


def exchange(x, is_odd, n):
    partner = swap_in_chip(x, n)
    r0 = jnp.where(is_odd, partner, x)
    r1 = jnp.where(is_odd, x, partner)
    up = jnp.concatenate([r1[1:], r0[2:]], axis=0)
    down = jnp.concatenate([r0[:6], r1[:5]], axis=0)
    near = [(i, (i + 1) % n) if i % 2 else (i, (i - 1) % n) for i in range(n)]
    far = [(i, (i - 3) % n) if i % 2 else (i, (i + 3) % n) for i in range(n)]
    got1 = lax.ppermute(jnp.where(is_odd, up, down), AXES, near)
    fwd_up = jnp.concatenate([got1[2:6], got1[8:11]], axis=0)
    fwd_down = jnp.concatenate([got1[0:4], got1[6:9]], axis=0)
    got2 = lax.ppermute(jnp.where(is_odd, fwd_down, fwd_up), AXES, far)
    fwd_up = jnp.concatenate([got2[2:4], got2[6:7]], axis=0)
    fwd_down = jnp.concatenate([got2[0:2], got2[4:5]], axis=0)
    got3 = lax.ppermute(jnp.where(is_odd, fwd_up, fwd_down), AXES, near)
    mine = jnp.concatenate([got1, got2, got3], axis=0)
    other = swap_in_chip(mine, n)
    a = jnp.concatenate([mine[0:11], other[11:18], mine[18:21]], axis=0)
    b = jnp.concatenate([other[0:11], mine[11:18], other[18:21]], axis=0)
    from_below_chips = jnp.where(is_odd, b, a)
    from_above_chips = jnp.where(is_odd, a, b)
    return r0, r1, from_below_chips, from_above_chips


def block_source(k, o, w, r0, r1, lower, upper):
    q = k + o
    if q == 0:
        return r0[w]
    if q == 1:
        return r1[w]
    if q < 0:
        d = (-q + 1) // 2
        base = FLOW_BASE[d]
        if -q % 2 == 1:
            return lower[base + w - (2 * d - 1)]
        return lower[base + (8 - 2 * d) + w - 2 * d]
    d = q // 2
    base = FLOW_BASE[d]
    if q % 2 == 0:
        return upper[base + w]
    return upper[base + (8 - 2 * d) + w]


def fetch_rows(x, is_odd, n):
    r0, r1, lower, upper = exchange(x, is_odd, n)

    def gather(k, sign):
        blocks = []
        for d in range(1, REACH + 1):
            widths = range(d, WIDTH) if sign < 0 else range(WIDTH - d)
            blocks += [block_source(k, sign * d, w, r0, r1, lower, upper) for w in widths]
        return jnp.stack(blocks, axis=0)

    above = jnp.where(is_odd, gather(1, -1), gather(0, -1))
    below = jnp.where(is_odd, gather(1, 1), gather(0, 1))
    rows_above, rows_below = [], []
    start = 0
    for d in range(1, REACH + 1):
        rows_above.append(above[start:start + WIDTH - d])
        rows_below.append(below[start:start + WIDTH - d])
        start += WIDTH - d
    return rows_above, rows_below


def make_upper(local_band, rows_above, rows_below):

    def upper_block(offset, width):
        if offset == 0:
            return local_band[width]
        if offset < 0:
            return rows_above[-offset - 1][width + offset]
        return rows_below[offset - 1][width]

    return upper_block


def left_operand(upper_block, inner):
    if inner >= 0:
        return (upper_block(0, inner), 1)
    return (upper_block(inner, -inner), 0)


def right_operand(upper_block, inner, target):
    if target >= inner:
        return (upper_block(inner, target - inner), 0)
    return (upper_block(target, inner - target), 1)


def band_product(upper_left, upper_right):
    results = []
    for target in range(REACH + 1):
        total = None
        for inner in range(target - REACH, REACH + 1):
            left_block, left_dim = left_operand(upper_left, inner)
            right_block, right_dim = right_operand(upper_right, inner, target)
            term = lax.dot_general(
                left_block,
                right_block,
                (((left_dim,), (right_dim,)), ((), ())),
                precision=lax.Precision.HIGHEST,
                preferred_element_type=jnp.float32,
            )
            total = term if total is None else total + term
        results.append(total)
    return jnp.stack(results, axis=0)


def on_device(density, pattern):
    local_band = density[0]
    n = lax.axis_size("row") * lax.axis_size("col")
    position = lax.axis_index("row") * lax.axis_size("col") + lax.axis_index("col")
    is_odd = (position % 2) == 1
    columns = (position + jnp.arange(WIDTH, dtype=jnp.int32)) % n
    flags = jnp.any(pattern[0][None, :] == columns[:, None], axis=1).astype(jnp.float32)[
        :, None, None
    ]
    above_p, below_p = fetch_rows(local_band, is_odd, n)
    upper_p = make_upper(local_band, above_p, below_p)
    square = flags * band_product(upper_p, upper_p)
    above_s, below_s = fetch_rows(square, is_odd, n)
    upper_s = make_upper(square, above_s, below_s)
    cube = flags * band_product(upper_p, upper_s)
    return (3.0 * square - 2.0 * cube)[None]


def solution(mesh):
    return jax.shard_map(
        on_device,
        mesh=mesh,
        in_specs=(P(AXES, None, None, None), P(AXES, None)),
        out_specs=P(AXES, None, None, None),
        check_vma=False,
    )
```

```python
import jax
import jax.numpy as jnp
from jax import lax
from jax.experimental import pallas as pl
from jax.experimental.pallas import tpu as pltpu
from jax.sharding import PartitionSpec as P

REACH = 6
WIDTH = REACH + 1
AXES = ("row", "col")
CHIPS_OUT = 3
INTERPRET = False
FLOW_BASE = {1: 0, 2: 11, 3: 18}


def swap_in_chip(x, n):
    return lax.ppermute(x, AXES, [(i, i ^ 1) for i in range(n)])


def exchange(x, is_odd, n):
    partner = swap_in_chip(x, n)
    r0 = jnp.where(is_odd, partner, x)
    r1 = jnp.where(is_odd, x, partner)
    received = []
    for d in range(1, CHIPS_OUT + 1):
        up = jnp.concatenate([r1[2 * d - 1:], r0[2 * d:]], axis=0)
        down = jnp.concatenate([r0[: 8 - 2 * d], r1[: 7 - 2 * d]], axis=0)
        buf = jnp.where(is_odd, up, down)
        step = 2 * d - 1
        route = [(i, (i + step) % n) if i % 2 else (i, (i - step) % n) for i in range(n)]
        received.append(lax.ppermute(buf, AXES, route))
    got = jnp.concatenate(received, axis=0)
    other = swap_in_chip(got, n)
    from_below_chips = jnp.where(is_odd, other, got)
    from_above_chips = jnp.where(is_odd, got, other)
    return r0, r1, from_below_chips, from_above_chips


def block_source(k, o, w, r0, r1, lower, upper):
    q = k + o
    if q == 0:
        return r0[w]
    if q == 1:
        return r1[w]
    if q < 0:
        d = (-q + 1) // 2
        base = FLOW_BASE[d]
        if -q % 2 == 1:
            return lower[base + w - (2 * d - 1)]
        return lower[base + (8 - 2 * d) + w - 2 * d]
    d = q // 2
    base = FLOW_BASE[d]
    if q % 2 == 0:
        return upper[base + w]
    return upper[base + (8 - 2 * d) + w]


def fetch_rows(x, is_odd, n):
    r0, r1, lower, upper = exchange(x, is_odd, n)

    def gather(k, sign):
        blocks = []
        for d in range(1, REACH + 1):
            widths = range(d, WIDTH) if sign < 0 else range(WIDTH - d)
            blocks += [block_source(k, sign * d, w, r0, r1, lower, upper) for w in widths]
        return jnp.stack(blocks, axis=0)

    above = jnp.where(is_odd, gather(1, -1), gather(0, -1))
    below = jnp.where(is_odd, gather(1, 1), gather(0, 1))
    return above, below


def row_starts():
    starts, start = [], 0
    for d in range(1, REACH + 1):
        starts.append(start)
        start += WIDTH - d
    return starts


def band_kernel(lp, la, lb, rp, ra, rb, out):
    starts = row_starts()

    def upper(local, above, below, offset, width):
        if offset == 0:
            return local[width]
        if offset < 0:
            return above[starts[-offset - 1] + width + offset]
        return below[starts[offset - 1] + width]

    for target in range(WIDTH):
        total = None
        for inner in range(target - REACH, REACH + 1):
            if inner >= 0:
                left = upper(lp, la, lb, 0, inner)
            else:
                left = upper(lp, la, lb, inner, -inner).T
            if target >= inner:
                right, right_dim = upper(rp, ra, rb, inner, target - inner), 0
            else:
                right, right_dim = upper(rp, ra, rb, target, inner - target), 1
            term = lax.dot_general(
                left,
                right,
                (((1,), (right_dim,)), ((), ())),
                precision=lax.Precision.HIGHEST,
                preferred_element_type=jnp.float32,
            )
            total = term if total is None else total + term
        out[target] = total


def band_product(left, right):
    local = left[0]
    vmem = pl.BlockSpec(memory_space=pltpu.VMEM)
    return pl.pallas_call(
        band_kernel,
        out_shape=jax.ShapeDtypeStruct(local.shape, jnp.float32),
        in_specs=[vmem] * 6,
        out_specs=vmem,
        interpret=INTERPRET,
    )(*left, *right)


def on_device(density, pattern):
    local_band = density[0]
    n = lax.axis_size("row") * lax.axis_size("col")
    position = lax.axis_index("row") * lax.axis_size("col") + lax.axis_index("col")
    is_odd = (position % 2) == 1
    columns = (position + jnp.arange(WIDTH, dtype=jnp.int32)) % n
    flags = jnp.any(pattern[0][None, :] == columns[:, None], axis=1).astype(jnp.float32)[
        :, None, None
    ]
    above_p, below_p = fetch_rows(local_band, is_odd, n)
    band_p = (local_band, above_p, below_p)
    square = flags * band_product(band_p, band_p)
    above_s, below_s = fetch_rows(square, is_odd, n)
    cube = flags * band_product(band_p, (square, above_s, below_s))
    return (3.0 * square - 2.0 * cube)[None]


def solution(mesh):
    return jax.shard_map(
        on_device,
        mesh=mesh,
        in_specs=(P(AXES, None, None, None), P(AXES, None)),
        out_specs=P(AXES, None, None, None),
        check_vma=False,
    )
```

```python
import functools

import jax
import jax.numpy as jnp
from jax import lax
from jax.experimental import pallas as pl
from jax.experimental.pallas import tpu as pltpu
from jax.sharding import PartitionSpec as P

REACH = 6
WIDTH = REACH + 1
AXES = ("row", "col")
CHIPS_OUT = 3
INTERPRET = False
FLOW_BASE = {1: 0, 2: 11, 3: 18}


def swap_in_chip(x, n):
    return lax.ppermute(x, AXES, [(i, i ^ 1) for i in range(n)])


def block_source(k, o, w, r0, r1, lower, upper):
    q = k + o
    if q == 0:
        return r0[w]
    if q == 1:
        return r1[w]
    if q < 0:
        d = (-q + 1) // 2
        base = FLOW_BASE[d]
        if -q % 2 == 1:
            return lower[base + w - (2 * d - 1)]
        return lower[base + (8 - 2 * d) + w - 2 * d]
    d = q // 2
    base = FLOW_BASE[d]
    if q % 2 == 0:
        return upper[base + w]
    return upper[base + (8 - 2 * d) + w]


def chip_refs(k, own, partner, got, other):
    if k == 0:
        return own, partner, got, other
    return partner, own, other, got


def band_kernel(parity, flags, lx, lp, lg, lo, rx, rp, rg, ro, out, *, final):
    def compute(k):
        left = chip_refs(k, lx, lp, lg, lo)
        right = chip_refs(k, rx, rp, rg, ro)
        for target in range(WIDTH):
            total = None
            for inner in range(target - REACH, REACH + 1):
                if inner >= 0:
                    a = block_source(k, 0, inner, *left)
                else:
                    a = block_source(k, inner, -inner, *left).T
                if target >= inner:
                    b, b_dim = block_source(k, inner, target - inner, *right), 0
                else:
                    b, b_dim = block_source(k, target, inner - target, *right), 1
                term = lax.dot_general(
                    a,
                    b,
                    (((1,), (b_dim,)), ((), ())),
                    precision=lax.Precision.HIGHEST,
                    preferred_element_type=jnp.float32,
                )
                total = term if total is None else total + term
            total = flags[target] * total
            if final:
                total = 3.0 * rx[target] - 2.0 * total
            out[target] = total

    for k in (0, 1):
        pl.when(parity[0] == k)(lambda k=k: compute(k))


def band_product(parity, flags, left, right, final):
    vmem = pl.BlockSpec(memory_space=pltpu.VMEM)
    smem = pl.BlockSpec(memory_space=pltpu.SMEM)
    local = left[0]
    return pl.pallas_call(
        functools.partial(band_kernel, final=final),
        out_shape=jax.ShapeDtypeStruct(local.shape, jnp.float32),
        in_specs=[smem, smem] + [vmem] * 8,
        out_specs=vmem,
        interpret=INTERPRET,
    )(parity, flags, *left, *right)


def exchange_rows(x, is_odd, n):
    partner = swap_in_chip(x, n)
    r0 = jnp.where(is_odd, partner, x)
    r1 = jnp.where(is_odd, x, partner)
    received = []
    for d in range(1, CHIPS_OUT + 1):
        up = jnp.concatenate([r1[2 * d - 1:], r0[2 * d:]], axis=0)
        down = jnp.concatenate([r0[: 8 - 2 * d], r1[: 7 - 2 * d]], axis=0)
        buf = jnp.where(is_odd, up, down)
        step = 2 * d - 1
        route = [(i, (i + step) % n) if i % 2 else (i, (i - step) % n) for i in range(n)]
        received.append(lax.ppermute(buf, AXES, route))
    got = jnp.concatenate(received, axis=0)
    other = swap_in_chip(got, n)
    return (x, partner, got, other)


def on_device(density, pattern):
    local_band = density[0]
    n = lax.axis_size("row") * lax.axis_size("col")
    position = lax.axis_index("row") * lax.axis_size("col") + lax.axis_index("col")
    is_odd = (position % 2) == 1
    parity = (position % 2).astype(jnp.int32).reshape(1)
    columns = (position + jnp.arange(WIDTH, dtype=jnp.int32)) % n
    flags = jnp.any(pattern[0][None, :] == columns[:, None], axis=1).astype(jnp.float32)
    chip_p = exchange_rows(local_band, is_odd, n)
    square = band_product(parity, flags, chip_p, chip_p, final=False)
    chip_s = exchange_rows(square, is_odd, n)
    purified = band_product(parity, flags, chip_p, chip_s, final=True)
    return purified[None]


def solution(mesh):
    return jax.shard_map(
        on_device,
        mesh=mesh,
        in_specs=(P(AXES, None, None, None), P(AXES, None)),
        out_specs=P(AXES, None, None, None),
        check_vma=False,
    )
```

```python
import functools

import jax
import jax.numpy as jnp
from jax import lax
from jax.experimental import pallas as pl
from jax.experimental.pallas import tpu as pltpu
from jax.sharding import PartitionSpec as P

REACH = 6
WIDTH = REACH + 1
AXES = ("row", "col")
CHIPS_OUT = 3
INTERPRET = False
FLOW_BASE = {1: 0, 2: 11, 3: 18}


def swap_in_chip(x, n):
    return lax.ppermute(x, AXES, [(i, i ^ 1) for i in range(n)])


def block_source(k, o, w, r0, r1, lower, upper):
    q = k + o
    if q == 0:
        return r0[w]
    if q == 1:
        return r1[w]
    if q < 0:
        d = (-q + 1) // 2
        base = FLOW_BASE[d]
        if -q % 2 == 1:
            return lower[base + w - (2 * d - 1)]
        return lower[base + (8 - 2 * d) + w - 2 * d]
    d = q // 2
    base = FLOW_BASE[d]
    if q % 2 == 0:
        return upper[base + w]
    return upper[base + (8 - 2 * d) + w]


def chip_refs(k, own, partner, got, other):
    if k == 0:
        return own, partner, got, other
    return partner, own, other, got


def split(x):
    hi = x.astype(jnp.bfloat16)
    lo = (x - hi.astype(jnp.float32)).astype(jnp.bfloat16)
    return hi, lo


def product(a_hi, a_lo, b, b_dim):
    b_hi, b_lo = split(b)
    dims = (((1,), (b_dim,)), ((), ()))

    def dot(x, y):
        return lax.dot_general(x, y, dims, preferred_element_type=jnp.float32)

    return dot(a_hi, b_hi) + (dot(a_hi, b_lo) + dot(a_lo, b_hi))


def band_kernel(parity, flags, lx, lp, lg, lo, rx, rp, rg, ro, out, left_hi, left_lo, *, final):
    def compute(k):
        left = chip_refs(k, lx, lp, lg, lo)
        right = chip_refs(k, rx, rp, rg, ro)
        for inner in range(-REACH, REACH + 1):
            if inner >= 0:
                a = block_source(k, 0, inner, *left)
            else:
                a = block_source(k, inner, -inner, *left).T
            a_hi, a_lo = split(a)
            left_hi[inner + REACH] = a_hi
            left_lo[inner + REACH] = a_lo
        for target in range(WIDTH):
            total = None
            for inner in range(target - REACH, REACH + 1):
                if target >= inner:
                    b, b_dim = block_source(k, inner, target - inner, *right), 0
                else:
                    b, b_dim = block_source(k, target, inner - target, *right), 1
                term = product(left_hi[inner + REACH], left_lo[inner + REACH], b, b_dim)
                total = term if total is None else total + term
            total = flags[target] * total
            if final:
                total = 3.0 * rx[target] - 2.0 * total
            out[target] = total

    for k in (0, 1):
        pl.when(parity[0] == k)(lambda k=k: compute(k))


def band_product(parity, flags, left, right, final):
    vmem = pl.BlockSpec(memory_space=pltpu.VMEM)
    smem = pl.BlockSpec(memory_space=pltpu.SMEM)
    local = left[0]
    b = local.shape[-1]
    return pl.pallas_call(
        functools.partial(band_kernel, final=final),
        out_shape=jax.ShapeDtypeStruct(local.shape, jnp.float32),
        in_specs=[smem, smem] + [vmem] * 8,
        out_specs=vmem,
        scratch_shapes=[pltpu.VMEM((2 * REACH + 1, b, b), jnp.bfloat16)] * 2,
        interpret=INTERPRET,
    )(parity, flags, *left, *right)


def exchange_rows(x, is_odd, n):
    partner = swap_in_chip(x, n)
    r0 = jnp.where(is_odd, partner, x)
    r1 = jnp.where(is_odd, x, partner)
    received = []
    for d in range(1, CHIPS_OUT + 1):
        up = jnp.concatenate([r1[2 * d - 1:], r0[2 * d:]], axis=0)
        down = jnp.concatenate([r0[: 8 - 2 * d], r1[: 7 - 2 * d]], axis=0)
        buf = jnp.where(is_odd, up, down)
        step = 2 * d - 1
        route = [(i, (i + step) % n) if i % 2 else (i, (i - step) % n) for i in range(n)]
        received.append(lax.ppermute(buf, AXES, route))
    got = jnp.concatenate(received, axis=0)
    other = swap_in_chip(got, n)
    return (x, partner, got, other)


def on_device(density, pattern):
    local_band = density[0]
    n = lax.axis_size("row") * lax.axis_size("col")
    position = lax.axis_index("row") * lax.axis_size("col") + lax.axis_index("col")
    is_odd = (position % 2) == 1
    parity = (position % 2).astype(jnp.int32).reshape(1)
    columns = (position + jnp.arange(WIDTH, dtype=jnp.int32)) % n
    flags = jnp.any(pattern[0][None, :] == columns[:, None], axis=1).astype(jnp.float32)
    chip_p = exchange_rows(local_band, is_odd, n)
    square = band_product(parity, flags, chip_p, chip_p, final=False)
    chip_s = exchange_rows(square, is_odd, n)
    purified = band_product(parity, flags, chip_p, chip_s, final=True)
    return purified[None]


def solution(mesh):
    return jax.shard_map(
        on_device,
        mesh=mesh,
        in_specs=(P(AXES, None, None, None), P(AXES, None)),
        out_specs=P(AXES, None, None, None),
        check_vma=False,
    )
```

```python
import functools

import jax
import jax.numpy as jnp
from jax import lax
from jax.experimental import pallas as pl
from jax.experimental.pallas import tpu as pltpu
from jax.sharding import PartitionSpec as P

REACH = 6
WIDTH = REACH + 1
AXES = ("row", "col")
CHIPS_OUT = 3
INTERPRET = False
FLOW_BASE = {1: 0, 2: 11, 3: 18}


def swap_in_chip(x, n):
    return lax.ppermute(x, AXES, [(i, i ^ 1) for i in range(n)])


def block_source(k, o, w, r0, r1, lower, upper):
    q = k + o
    if q == 0:
        return r0[w]
    if q == 1:
        return r1[w]
    if q < 0:
        d = (-q + 1) // 2
        base = FLOW_BASE[d]
        if -q % 2 == 1:
            return lower[base + w - (2 * d - 1)]
        return lower[base + (8 - 2 * d) + w - 2 * d]
    d = q // 2
    base = FLOW_BASE[d]
    if q % 2 == 0:
        return upper[base + w]
    return upper[base + (8 - 2 * d) + w]


def chip_refs(k, own, partner, got, other):
    if k == 0:
        return own, partner, got, other
    return partner, own, other, got


def split(x):
    hi = x.astype(jnp.bfloat16)
    lo = (x - hi.astype(jnp.float32)).astype(jnp.bfloat16)
    return hi, lo


def band_kernel(parity, flags, lx, lp, lg, lo, rx, rp, rg, ro, out, left_all, right_all, *, final):
    b = out.shape[-1]

    def compute(k):
        left = chip_refs(k, lx, lp, lg, lo)
        right = chip_refs(k, rx, rp, rg, ro)
        for inner in range(-REACH, REACH + 1):
            if inner >= 0:
                a = block_source(k, 0, inner, *left)
            else:
                a = block_source(k, inner, -inner, *left).T
            a_hi, a_lo = split(a)
            i = 3 * (inner + REACH)
            left_all[:, i * b:(i + 1) * b] = a_hi
            left_all[:, (i + 1) * b:(i + 2) * b] = a_hi
            left_all[:, (i + 2) * b:(i + 3) * b] = a_lo
        for target in range(WIDTH):
            rows = right_all.at[target % 2]
            for j, inner in enumerate(range(target - REACH, REACH + 1)):
                if target >= inner:
                    m = block_source(k, inner, target - inner, *right)
                else:
                    m = block_source(k, target, inner - target, *right).T
                m_hi, m_lo = split(m)
                rows[3 * j * b:(3 * j + 1) * b, :] = m_hi
                rows[(3 * j + 1) * b:(3 * j + 2) * b, :] = m_lo
                rows[(3 * j + 2) * b:(3 * j + 3) * b, :] = m_hi
            depth = 3 * (2 * REACH + 1 - target) * b
            total = jnp.dot(
                left_all[:, 3 * target * b:],
                rows[:depth, :],
                preferred_element_type=jnp.float32,
            )
            total = flags[target] * total
            if final:
                total = 3.0 * rx[target] - 2.0 * total
            out[target] = total

    for k in (0, 1):
        pl.when(parity[0] == k)(lambda k=k: compute(k))


def band_product(parity, flags, left, right, final):
    vmem = pl.BlockSpec(memory_space=pltpu.VMEM)
    smem = pl.BlockSpec(memory_space=pltpu.SMEM)
    local = left[0]
    b = local.shape[-1]
    depth = 3 * (2 * REACH + 1) * b
    return pl.pallas_call(
        functools.partial(band_kernel, final=final),
        out_shape=jax.ShapeDtypeStruct(local.shape, jnp.float32),
        in_specs=[smem, smem] + [vmem] * 8,
        out_specs=vmem,
        scratch_shapes=[
            pltpu.VMEM((b, depth), jnp.bfloat16),
            pltpu.VMEM((2, depth, b), jnp.bfloat16),
        ],
        interpret=INTERPRET,
    )(parity, flags, *left, *right)


def exchange_rows(x, is_odd, n):
    partner = swap_in_chip(x, n)
    r0 = jnp.where(is_odd, partner, x)
    r1 = jnp.where(is_odd, x, partner)
    received = []
    for d in range(1, CHIPS_OUT + 1):
        up = jnp.concatenate([r1[2 * d - 1:], r0[2 * d:]], axis=0)
        down = jnp.concatenate([r0[: 8 - 2 * d], r1[: 7 - 2 * d]], axis=0)
        buf = jnp.where(is_odd, up, down)
        step = 2 * d - 1
        route = [(i, (i + step) % n) if i % 2 else (i, (i - step) % n) for i in range(n)]
        received.append(lax.ppermute(buf, AXES, route))
    got = jnp.concatenate(received, axis=0)
    other = swap_in_chip(got, n)
    return (x, partner, got, other)


def on_device(density, pattern):
    local_band = density[0]
    n = lax.axis_size("row") * lax.axis_size("col")
    position = lax.axis_index("row") * lax.axis_size("col") + lax.axis_index("col")
    is_odd = (position % 2) == 1
    parity = (position % 2).astype(jnp.int32).reshape(1)
    columns = (position + jnp.arange(WIDTH, dtype=jnp.int32)) % n
    flags = jnp.any(pattern[0][None, :] == columns[:, None], axis=1).astype(jnp.float32)
    chip_p = exchange_rows(local_band, is_odd, n)
    square = band_product(parity, flags, chip_p, chip_p, final=False)
    chip_s = exchange_rows(square, is_odd, n)
    purified = band_product(parity, flags, chip_p, chip_s, final=True)
    return purified[None]


def solution(mesh):
    return jax.shard_map(
        on_device,
        mesh=mesh,
        in_specs=(P(AXES, None, None, None), P(AXES, None)),
        out_specs=P(AXES, None, None, None),
        check_vma=False,
    )
```

```python
import functools

import jax
import jax.numpy as jnp
from jax import lax
from jax.experimental import pallas as pl
from jax.experimental.pallas import tpu as pltpu
from jax.sharding import PartitionSpec as P

REACH = 6
WIDTH = REACH + 1
AXES = ("row", "col")
CHIPS_OUT = 3
INTERPRET = False
FLOW_BASE = {1: 0, 2: 11, 3: 18}


def swap_in_chip(x, n):
    return lax.ppermute(x, AXES, [(i, i ^ 1) for i in range(n)])


def block_source(k, o, w, r0, r1, lower, upper):
    q = k + o
    if q == 0:
        return r0[w]
    if q == 1:
        return r1[w]
    if q < 0:
        d = (-q + 1) // 2
        base = FLOW_BASE[d]
        if -q % 2 == 1:
            return lower[base + w - (2 * d - 1)]
        return lower[base + (8 - 2 * d) + w - 2 * d]
    d = q // 2
    base = FLOW_BASE[d]
    if q % 2 == 0:
        return upper[base + w]
    return upper[base + (8 - 2 * d) + w]


def chip_refs(k, own, partner, got, other):
    if k == 0:
        return own, partner, got, other
    return partner, own, other, got


def block_level(k, o):
    q = k + o
    if q in (0, 1):
        return 0
    from_lower_chip = q < 0
    return 1 + int(from_lower_chip == (k == 1))


def term_blocks(k, inner, target):
    left = (0, inner, False) if inner >= 0 else (inner, -inner, True)
    if target >= inner:
        right = (inner, target - inner, 0)
    else:
        right = (target, inner - target, 1)
    level = max(block_level(k, left[0]), block_level(k, right[0]))
    return left, right, level


def split(x):
    hi = x.astype(jnp.bfloat16)
    lo = (x - hi.astype(jnp.float32)).astype(jnp.bfloat16)
    return hi, lo


def product(a_hi, a_lo, m, m_dim):
    m_hi, m_lo = split(m)
    dims = (((1,), (m_dim,)), ((), ()))

    def dot(x, y):
        return lax.dot_general(x, y, dims, preferred_element_type=jnp.float32)

    return dot(a_hi, m_hi) + (dot(a_hi, m_lo) + dot(a_lo, m_hi))


def band_kernel(*refs, level, final):
    count = 2 + level
    parity, flags = refs[0], refs[1]
    left_in = list(refs[2:2 + count]) + [None] * (4 - count)
    right_in = list(refs[2 + count:2 + 2 * count]) + [None] * (4 - count)
    rest = refs[2 + 2 * count:]
    partial = rest[0] if level > 0 else None
    out, left_hi, left_lo = rest[-3:]

    def compute(k):
        left = chip_refs(k, *left_in)
        right = chip_refs(k, *right_in)
        terms = {
            t: [i for i in range(t - REACH, REACH + 1) if term_blocks(k, i, t)[2] == level]
            for t in range(WIDTH)
        }
        used = sorted({i for t in terms for i in terms[t]})
        for inner in used:
            (o, w, transposed), _, _ = term_blocks(k, inner, 0 if inner < 0 else inner)
            a = block_source(k, o, w, *left)
            a_hi, a_lo = split(a.T if transposed else a)
            left_hi[inner + REACH] = a_hi
            left_lo[inner + REACH] = a_lo
        for target in range(WIDTH):
            total = None if partial is None else partial[target]
            for inner in terms[target]:
                _, (o, w, m_dim), _ = term_blocks(k, inner, target)
                m = block_source(k, o, w, *right)
                term = product(left_hi[inner + REACH], left_lo[inner + REACH], m, m_dim)
                total = term if total is None else total + term
            if total is None:
                total = jnp.zeros(out.shape[1:], jnp.float32)
            if level == 2:
                total = flags[target] * total
                if final:
                    total = 3.0 * right_in[0][target] - 2.0 * total
            out[target] = total

    for k in (0, 1):
        pl.when(parity[0] == k)(lambda k=k: compute(k))


def band_level(level, parity, flags, left, right, partial, final):
    vmem = pl.BlockSpec(memory_space=pltpu.VMEM)
    smem = pl.BlockSpec(memory_space=pltpu.SMEM)
    local = left[0]
    b = local.shape[-1]
    count = 2 + level
    arrays = list(left[:count]) + list(right[:count]) + ([partial] if level > 0 else [])
    return pl.pallas_call(
        functools.partial(band_kernel, level=level, final=final),
        out_shape=jax.ShapeDtypeStruct(local.shape, jnp.float32),
        in_specs=[smem, smem] + [vmem] * len(arrays),
        out_specs=vmem,
        scratch_shapes=[pltpu.VMEM((2 * REACH + 1, b, b), jnp.bfloat16)] * 2,
        interpret=INTERPRET,
    )(parity, flags, *arrays)


def band_product(parity, flags, left, right, final):
    partial = None
    for level in range(3):
        partial = band_level(level, parity, flags, left, right, partial, final)
    return partial


def exchange_rows(x, is_odd, n):
    partner = swap_in_chip(x, n)
    r0 = jnp.where(is_odd, partner, x)
    r1 = jnp.where(is_odd, x, partner)
    received = []
    for d in range(1, CHIPS_OUT + 1):
        up = jnp.concatenate([r1[2 * d - 1:], r0[2 * d:]], axis=0)
        down = jnp.concatenate([r0[: 8 - 2 * d], r1[: 7 - 2 * d]], axis=0)
        buf = jnp.where(is_odd, up, down)
        step = 2 * d - 1
        route = [(i, (i + step) % n) if i % 2 else (i, (i - step) % n) for i in range(n)]
        received.append(lax.ppermute(buf, AXES, route))
    got = jnp.concatenate(received, axis=0)
    other = swap_in_chip(got, n)
    return (x, partner, got, other)


def on_device(density, pattern):
    local_band = density[0]
    n = lax.axis_size("row") * lax.axis_size("col")
    position = lax.axis_index("row") * lax.axis_size("col") + lax.axis_index("col")
    is_odd = (position % 2) == 1
    parity = (position % 2).astype(jnp.int32).reshape(1)
    columns = (position + jnp.arange(WIDTH, dtype=jnp.int32)) % n
    flags = jnp.any(pattern[0][None, :] == columns[:, None], axis=1).astype(jnp.float32)
    chip_p = exchange_rows(local_band, is_odd, n)
    square = band_product(parity, flags, chip_p, chip_p, final=False)
    chip_s = exchange_rows(square, is_odd, n)
    purified = band_product(parity, flags, chip_p, chip_s, final=True)
    return purified[None]


def solution(mesh):
    return jax.shard_map(
        on_device,
        mesh=mesh,
        in_specs=(P(AXES, None, None, None), P(AXES, None)),
        out_specs=P(AXES, None, None, None),
        check_vma=False,
    )
```

```python
import functools

import jax
import jax.numpy as jnp
from jax import lax
from jax.experimental import pallas as pl
from jax.experimental.pallas import tpu as pltpu
from jax.sharding import PartitionSpec as P

REACH = 6
WIDTH = REACH + 1
AXES = ("row", "col")
CHIPS_OUT = 3
INTERPRET = False
FLOW_BASE = {1: 0, 2: 11, 3: 18}


def swap_in_chip(x, n):
    return lax.ppermute(x, AXES, [(i, i ^ 1) for i in range(n)])


def block_source(k, o, w, r0, r1, lower, upper):
    q = k + o
    if q == 0:
        return r0[w]
    if q == 1:
        return r1[w]
    if q < 0:
        d = (-q + 1) // 2
        base = FLOW_BASE[d]
        if -q % 2 == 1:
            return lower[base + w - (2 * d - 1)]
        return lower[base + (8 - 2 * d) + w - 2 * d]
    d = q // 2
    base = FLOW_BASE[d]
    if q % 2 == 0:
        return upper[base + w]
    return upper[base + (8 - 2 * d) + w]


def chip_refs(k, own, partner, got, other):
    if k == 0:
        return own, partner, got, other
    return partner, own, other, got


def split(x):
    hi = x.astype(jnp.bfloat16)
    lo = (x - hi.astype(jnp.float32)).astype(jnp.bfloat16)
    return hi, lo


def band_kernel(*refs, final):
    parity, flags = refs[0], refs[1]
    if final:
        left_in, right_in = None, refs[3:7]
        out, right_all = refs[7], refs[8]
        left_all = refs[2]
    else:
        left_in = right_in = refs[2:6]
        out, left_all, right_all = refs[6], refs[7], refs[8]
    b = out.shape[-1]

    def compute(k):
        right = chip_refs(k, *right_in)
        if not final:
            left = chip_refs(k, *left_in)
            for inner in range(-REACH, REACH + 1):
                if inner >= 0:
                    a = block_source(k, 0, inner, *left)
                else:
                    a = block_source(k, inner, -inner, *left).T
                a_hi, a_lo = split(a)
                i = 3 * (inner + REACH)
                left_all[:, i * b:(i + 1) * b] = a_hi
                left_all[:, (i + 1) * b:(i + 2) * b] = a_hi
                left_all[:, (i + 2) * b:(i + 3) * b] = a_lo
        for target in range(WIDTH):
            rows = right_all.at[target % 2]
            for j, inner in enumerate(range(target - REACH, REACH + 1)):
                if target >= inner:
                    m = block_source(k, inner, target - inner, *right)
                else:
                    m = block_source(k, target, inner - target, *right).T
                m_hi, m_lo = split(m)
                rows[3 * j * b:(3 * j + 1) * b, :] = m_hi
                rows[(3 * j + 1) * b:(3 * j + 2) * b, :] = m_lo
                rows[(3 * j + 2) * b:(3 * j + 3) * b, :] = m_hi
            depth = 3 * (2 * REACH + 1 - target) * b
            total = jnp.dot(
                left_all[:, 3 * target * b:],
                rows[:depth, :],
                preferred_element_type=jnp.float32,
            )
            total = flags[target] * total
            if final:
                total = 3.0 * right_in[0][target] - 2.0 * total
            out[target] = total

    for k in (0, 1):
        pl.when(parity[0] == k)(lambda k=k: compute(k))


def band_call(parity, flags, arrays, final):
    vmem = pl.BlockSpec(memory_space=pltpu.VMEM)
    smem = pl.BlockSpec(memory_space=pltpu.SMEM)
    local = arrays[-4]
    b = local.shape[-1]
    depth = 3 * (2 * REACH + 1) * b
    square_shape = jax.ShapeDtypeStruct(local.shape, jnp.float32)
    left_shape = jax.ShapeDtypeStruct((b, depth), jnp.bfloat16)
    return pl.pallas_call(
        functools.partial(band_kernel, final=final),
        out_shape=square_shape if final else (square_shape, left_shape),
        in_specs=[smem, smem] + [vmem] * len(arrays),
        out_specs=vmem if final else (vmem, vmem),
        scratch_shapes=[pltpu.VMEM((2, depth, b), jnp.bfloat16)],
        interpret=INTERPRET,
    )(parity, flags, *arrays)


def exchange_rows(x, is_odd, n):
    partner = swap_in_chip(x, n)
    r0 = jnp.where(is_odd, partner, x)
    r1 = jnp.where(is_odd, x, partner)
    received = []
    for d in range(1, CHIPS_OUT + 1):
        up = jnp.concatenate([r1[2 * d - 1:], r0[2 * d:]], axis=0)
        down = jnp.concatenate([r0[: 8 - 2 * d], r1[: 7 - 2 * d]], axis=0)
        buf = jnp.where(is_odd, up, down)
        step = 2 * d - 1
        route = [(i, (i + step) % n) if i % 2 else (i, (i - step) % n) for i in range(n)]
        received.append(lax.ppermute(buf, AXES, route))
    got = jnp.concatenate(received, axis=0)
    other = swap_in_chip(got, n)
    return (x, partner, got, other)


def on_device(density, pattern):
    local_band = density[0]
    n = lax.axis_size("row") * lax.axis_size("col")
    position = lax.axis_index("row") * lax.axis_size("col") + lax.axis_index("col")
    is_odd = (position % 2) == 1
    parity = (position % 2).astype(jnp.int32).reshape(1)
    columns = (position + jnp.arange(WIDTH, dtype=jnp.int32)) % n
    flags = jnp.any(pattern[0][None, :] == columns[:, None], axis=1).astype(jnp.float32)
    chip_p = exchange_rows(local_band, is_odd, n)
    square, left_all = band_call(parity, flags, chip_p, final=False)
    chip_s = exchange_rows(square, is_odd, n)
    purified = band_call(parity, flags, (left_all,) + chip_s, final=True)
    return purified[None]


def solution(mesh):
    return jax.shard_map(
        on_device,
        mesh=mesh,
        in_specs=(P(AXES, None, None, None), P(AXES, None)),
        out_specs=P(AXES, None, None, None),
        check_vma=False,
    )
```

```python
import functools

import jax
import jax.numpy as jnp
from jax import lax
from jax.experimental import pallas as pl
from jax.experimental.pallas import tpu as pltpu
from jax.sharding import PartitionSpec as P

REACH = 6
WIDTH = REACH + 1
AXES = ("row", "col")
CHIPS_OUT = 3
INTERPRET = False
FLOW_BASE = {1: 0, 2: 11, 3: 18}


def swap_in_chip(x, n):
    return lax.ppermute(x, AXES, [(i, i ^ 1) for i in range(n)])


def block_source(k, o, w, r0, r1, lower, upper):
    q = k + o
    if q == 0:
        return r0[w]
    if q == 1:
        return r1[w]
    if q < 0:
        d = (-q + 1) // 2
        base = FLOW_BASE[d]
        if -q % 2 == 1:
            return lower[base + w - (2 * d - 1)]
        return lower[base + (8 - 2 * d) + w - 2 * d]
    d = q // 2
    base = FLOW_BASE[d]
    if q % 2 == 0:
        return upper[base + w]
    return upper[base + (8 - 2 * d) + w]


def chip_refs(k, own, partner, got, other):
    if k == 0:
        return own, partner, got, other
    return partner, own, other, got


def split(x):
    hi = x.astype(jnp.bfloat16)
    lo = (x - hi.astype(jnp.float32)).astype(jnp.bfloat16)
    return hi, lo


class Fetched:
    def __init__(self, copy, buffer):
        self.copy, self.buffer, self.ready = copy, buffer, False

    def wait(self):
        if not self.ready:
            self.copy.wait()
            self.ready = True

    def __getitem__(self, index):
        self.wait()
        return self.buffer[index]

    def slab(self):
        self.wait()
        return self.buffer


def band_kernel(*refs, final, count):
    parity, flags = refs[0], refs[1]
    inputs = refs[2:2 + count]
    outs = refs[2 + count:2 + count + (1 if final else 2)]
    scratch = refs[2 + count + len(outs):]
    right_all, buffers, sems = scratch[0], scratch[1:1 + count], scratch[1 + count]
    out = outs[0]
    b = out.shape[-1]
    copies = [pltpu.make_async_copy(inputs[i], buffers[i], sems.at[i]) for i in range(count)]
    for copy in copies:
        copy.start()

    def compute(k):
        fetched = [Fetched(copies[i], buffers[i]) for i in range(count)]
        if final:
            left_all = fetched[0]
            right_in = fetched[1:]
        else:
            left_all = outs[1]
            right_in = fetched
            left = chip_refs(k, *fetched)
            for inner in range(-REACH, REACH + 1):
                if inner >= 0:
                    a = block_source(k, 0, inner, *left)
                else:
                    a = block_source(k, inner, -inner, *left).T
                a_hi, a_lo = split(a)
                i = 3 * (inner + REACH)
                left_all[:, i * b:(i + 1) * b] = a_hi
                left_all[:, (i + 1) * b:(i + 2) * b] = a_hi
                left_all[:, (i + 2) * b:(i + 3) * b] = a_lo
        right = chip_refs(k, *right_in)
        for target in range(WIDTH):
            rows = right_all.at[target % 2]
            for j, inner in enumerate(range(target - REACH, REACH + 1)):
                if target >= inner:
                    m = block_source(k, inner, target - inner, *right)
                else:
                    m = block_source(k, target, inner - target, *right).T
                m_hi, m_lo = split(m)
                rows[3 * j * b:(3 * j + 1) * b, :] = m_hi
                rows[(3 * j + 1) * b:(3 * j + 2) * b, :] = m_lo
                rows[(3 * j + 2) * b:(3 * j + 3) * b, :] = m_hi
            depth = 3 * (2 * REACH + 1 - target) * b
            lhs = left_all.slab() if final else left_all
            total = jnp.dot(
                lhs[:, 3 * target * b:],
                rows[:depth, :],
                preferred_element_type=jnp.float32,
            )
            total = flags[target] * total
            if final:
                total = 3.0 * right_in[0][target] - 2.0 * total
            out[target] = total
        for f in fetched:
            f.wait()

    for k in (0, 1):
        pl.when(parity[0] == k)(lambda k=k: compute(k))


def band_call(parity, flags, arrays, final):
    vmem = pl.BlockSpec(memory_space=pltpu.VMEM)
    smem = pl.BlockSpec(memory_space=pltpu.SMEM)
    anywhere = pl.BlockSpec(memory_space=pl.ANY)
    local = arrays[-4]
    b = local.shape[-1]
    depth = 3 * (2 * REACH + 1) * b
    square_shape = jax.ShapeDtypeStruct(local.shape, jnp.float32)
    left_shape = jax.ShapeDtypeStruct((b, depth), jnp.bfloat16)
    count = len(arrays)
    return pl.pallas_call(
        functools.partial(band_kernel, final=final, count=count),
        out_shape=square_shape if final else (square_shape, left_shape),
        in_specs=[smem, smem] + [anywhere] * count,
        out_specs=vmem if final else (vmem, vmem),
        scratch_shapes=[pltpu.VMEM((2, depth, b), jnp.bfloat16)]
        + [pltpu.VMEM(a.shape, a.dtype) for a in arrays]
        + [pltpu.SemaphoreType.DMA((count,))],
        interpret=INTERPRET,
    )(parity, flags, *arrays)


def exchange_rows(x, is_odd, n):
    partner = swap_in_chip(x, n)
    r0 = jnp.where(is_odd, partner, x)
    r1 = jnp.where(is_odd, x, partner)
    received = []
    for d in range(1, CHIPS_OUT + 1):
        up = jnp.concatenate([r1[2 * d - 1:], r0[2 * d:]], axis=0)
        down = jnp.concatenate([r0[: 8 - 2 * d], r1[: 7 - 2 * d]], axis=0)
        buf = jnp.where(is_odd, up, down)
        step = 2 * d - 1
        route = [(i, (i + step) % n) if i % 2 else (i, (i - step) % n) for i in range(n)]
        received.append(lax.ppermute(buf, AXES, route))
    got = jnp.concatenate(received, axis=0)
    other = swap_in_chip(got, n)
    return (x, partner, got, other)


def on_device(density, pattern):
    local_band = density[0]
    n = lax.axis_size("row") * lax.axis_size("col")
    position = lax.axis_index("row") * lax.axis_size("col") + lax.axis_index("col")
    is_odd = (position % 2) == 1
    parity = (position % 2).astype(jnp.int32).reshape(1)
    columns = (position + jnp.arange(WIDTH, dtype=jnp.int32)) % n
    flags = jnp.any(pattern[0][None, :] == columns[:, None], axis=1).astype(jnp.float32)
    chip_p = exchange_rows(local_band, is_odd, n)
    square, left_all = band_call(parity, flags, chip_p, final=False)
    chip_s = exchange_rows(square, is_odd, n)
    purified = band_call(parity, flags, (left_all,) + chip_s, final=True)
    return purified[None]


def solution(mesh):
    return jax.shard_map(
        on_device,
        mesh=mesh,
        in_specs=(P(AXES, None, None, None), P(AXES, None)),
        out_specs=P(AXES, None, None, None),
        check_vma=False,
    )
```

```python
import functools

import jax
import jax.numpy as jnp
from jax import lax
from jax.experimental import pallas as pl
from jax.experimental.pallas import tpu as pltpu
from jax.sharding import PartitionSpec as P

REACH = 6
WIDTH = REACH + 1
AXES = ("row", "col")
CHIPS_OUT = 3
INTERPRET = False
FLOW_BASE = {1: 0, 2: 11, 3: 18}


def swap_in_chip(x, n):
    return lax.ppermute(x, AXES, [(i, i ^ 1) for i in range(n)])


def block_source(k, o, w, r0, r1, lower, upper):
    q = k + o
    if q == 0:
        return r0[w]
    if q == 1:
        return r1[w]
    if q < 0:
        d = (-q + 1) // 2
        base = FLOW_BASE[d]
        if -q % 2 == 1:
            return lower[base + w - (2 * d - 1)]
        return lower[base + (8 - 2 * d) + w - 2 * d]
    d = q // 2
    base = FLOW_BASE[d]
    if q % 2 == 0:
        return upper[base + w]
    return upper[base + (8 - 2 * d) + w]


KEPT = {
    0: ((1, 6), (7, 11), (12, 15), (16, 18), (19, 20)),
    1: ((0, 5), (6, 10), (11, 14), (15, 17), (18, 19)),
}


class Trimmed:
    def __init__(self, ref, sender):
        self.ref, self.where = ref, {}
        slot = 0
        for start, stop in KEPT[sender]:
            for full in range(start, stop):
                self.where[full] = slot
                slot += 1

    def __getitem__(self, full):
        return self.ref[self.where[full]]


def chip_refs(k, own, partner, got, other):
    other = Trimmed(other, 1 - k)
    if k == 0:
        return own, partner, got, other
    return partner, own, other, got


def split(x):
    hi = x.astype(jnp.bfloat16)
    lo = (x - hi.astype(jnp.float32)).astype(jnp.bfloat16)
    return hi, lo


def band_kernel(*refs, final):
    parity, flags = refs[0], refs[1]
    if final:
        left_in, right_in = None, refs[3:7]
        out, right_all = refs[7], refs[8]
        left_all = refs[2]
    else:
        left_in = right_in = refs[2:6]
        out, left_all, right_all = refs[6], refs[7], refs[8]
    b = out.shape[-1]

    def compute(k):
        right = chip_refs(k, *right_in)
        if not final:
            left = chip_refs(k, *left_in)
            for inner in range(-REACH, REACH + 1):
                if inner >= 0:
                    a = block_source(k, 0, inner, *left)
                else:
                    a = block_source(k, inner, -inner, *left).T
                a_hi, a_lo = split(a)
                i = 3 * (inner + REACH)
                left_all[:, i * b:(i + 1) * b] = a_hi
                left_all[:, (i + 1) * b:(i + 2) * b] = a_hi
                left_all[:, (i + 2) * b:(i + 3) * b] = a_lo
        for target in range(WIDTH):
            rows = right_all.at[target % 2]
            for j, inner in enumerate(range(target - REACH, REACH + 1)):
                if target >= inner:
                    m = block_source(k, inner, target - inner, *right)
                else:
                    m = block_source(k, target, inner - target, *right).T
                m_hi, m_lo = split(m)
                rows[3 * j * b:(3 * j + 1) * b, :] = m_hi
                rows[(3 * j + 1) * b:(3 * j + 2) * b, :] = m_lo
                rows[(3 * j + 2) * b:(3 * j + 3) * b, :] = m_hi
            depth = 3 * (2 * REACH + 1 - target) * b
            total = jnp.dot(
                left_all[:, 3 * target * b:],
                rows[:depth, :],
                preferred_element_type=jnp.float32,
            )
            total = flags[target] * total
            if final:
                total = 3.0 * right_in[0][target] - 2.0 * total
            out[target] = total

    for k in (0, 1):
        pl.when(parity[0] == k)(lambda k=k: compute(k))


def band_call(parity, flags, arrays, final):
    vmem = pl.BlockSpec(memory_space=pltpu.VMEM)
    smem = pl.BlockSpec(memory_space=pltpu.SMEM)
    local = arrays[-4]
    b = local.shape[-1]
    depth = 3 * (2 * REACH + 1) * b
    square_shape = jax.ShapeDtypeStruct(local.shape, jnp.float32)
    left_shape = jax.ShapeDtypeStruct((b, depth), jnp.bfloat16)
    return pl.pallas_call(
        functools.partial(band_kernel, final=final),
        out_shape=square_shape if final else (square_shape, left_shape),
        in_specs=[smem, smem] + [vmem] * len(arrays),
        out_specs=vmem if final else (vmem, vmem),
        scratch_shapes=[pltpu.VMEM((2, depth, b), jnp.bfloat16)],
        interpret=INTERPRET,
    )(parity, flags, *arrays)


def exchange_rows(x, is_odd, n):
    partner = swap_in_chip(x, n)
    r0 = jnp.where(is_odd, partner, x)
    r1 = jnp.where(is_odd, x, partner)
    received = []
    for d in range(1, CHIPS_OUT + 1):
        up = jnp.concatenate([r1[2 * d - 1:], r0[2 * d:]], axis=0)
        down = jnp.concatenate([r0[: 8 - 2 * d], r1[: 7 - 2 * d]], axis=0)
        buf = jnp.where(is_odd, up, down)
        step = 2 * d - 1
        route = [(i, (i + step) % n) if i % 2 else (i, (i - step) % n) for i in range(n)]
        received.append(lax.ppermute(buf, AXES, route))
    got = jnp.concatenate(received, axis=0)

    def kept(sender):
        return jnp.concatenate([got[a:b] for a, b in KEPT[sender]], axis=0)

    other = swap_in_chip(jnp.where(is_odd, kept(1), kept(0)), n)
    return (x, partner, got, other)


def on_device(density, pattern):
    local_band = density[0]
    n = lax.axis_size("row") * lax.axis_size("col")
    position = lax.axis_index("row") * lax.axis_size("col") + lax.axis_index("col")
    is_odd = (position % 2) == 1
    parity = (position % 2).astype(jnp.int32).reshape(1)
    columns = (position + jnp.arange(WIDTH, dtype=jnp.int32)) % n
    flags = jnp.any(pattern[0][None, :] == columns[:, None], axis=1).astype(jnp.float32)
    chip_p = exchange_rows(local_band, is_odd, n)
    square, left_all = band_call(parity, flags, chip_p, final=False)
    chip_s = exchange_rows(square, is_odd, n)
    purified = band_call(parity, flags, (left_all,) + chip_s, final=True)
    return purified[None]


def solution(mesh):
    return jax.shard_map(
        on_device,
        mesh=mesh,
        in_specs=(P(AXES, None, None, None), P(AXES, None)),
        out_specs=P(AXES, None, None, None),
        check_vma=False,
    )
```

```python
import functools

import jax
import jax.numpy as jnp
from jax import lax
from jax.experimental import pallas as pl
from jax.experimental.pallas import tpu as pltpu
from jax.sharding import PartitionSpec as P

REACH = 6
WIDTH = REACH + 1
AXES = ("row", "col")
CHIPS_OUT = 3
INTERPRET = False
FLOW_BASE = {1: 0, 2: 11, 3: 18}


def swap_in_chip(x, n):
    return lax.ppermute(x, AXES, [(i, i ^ 1) for i in range(n)])


def block_source(k, o, w, r0, r1, lower, upper):
    q = k + o
    if q == 0:
        return r0[w]
    if q == 1:
        return r1[w]
    if q < 0:
        d = (-q + 1) // 2
        base = FLOW_BASE[d]
        if -q % 2 == 1:
            return lower[base + w - (2 * d - 1)]
        return lower[base + (8 - 2 * d) + w - 2 * d]
    d = q // 2
    base = FLOW_BASE[d]
    if q % 2 == 0:
        return upper[base + w]
    return upper[base + (8 - 2 * d) + w]


KEPT = {
    0: ((1, 6), (7, 11), (12, 15), (16, 18), (19, 20)),
    1: ((0, 5), (6, 10), (11, 14), (15, 17), (18, 19)),
}


class Trimmed:
    def __init__(self, ref, sender):
        self.ref, self.where = ref, {}
        slot = 0
        for start, stop in KEPT[sender]:
            for full in range(start, stop):
                self.where[full] = slot
                slot += 1

    def __getitem__(self, full):
        return self.ref[self.where[full]]


class Shifted:
    def __init__(self, ref, first):
        self.ref, self.first = ref, first

    def __getitem__(self, w):
        assert self.first <= w < self.first + WIDTH - 1
        return self.ref[w - self.first]


def chip_refs(k, own, partner, got, other):
    other = Trimmed(other, 1 - k)
    partner = Shifted(partner, k)
    if k == 0:
        return own, partner, got, other
    return partner, own, other, got


def split(x):
    hi = x.astype(jnp.bfloat16)
    lo = (x - hi.astype(jnp.float32)).astype(jnp.bfloat16)
    return hi, lo


def band_kernel(*refs, final):
    parity, flags = refs[0], refs[1]
    if final:
        left_in, right_in = None, refs[3:7]
        out, right_all = refs[7], refs[8]
        left_all = refs[2]
    else:
        left_in = right_in = refs[2:6]
        out, left_all, right_all = refs[6], refs[7], refs[8]
    b = out.shape[-1]

    def compute(k):
        right = chip_refs(k, *right_in)
        if not final:
            left = chip_refs(k, *left_in)
            for inner in range(-REACH, REACH + 1):
                if inner >= 0:
                    a = block_source(k, 0, inner, *left)
                else:
                    a = block_source(k, inner, -inner, *left).T
                a_hi, a_lo = split(a)
                i = 3 * (inner + REACH)
                left_all[:, i * b:(i + 1) * b] = a_hi
                left_all[:, (i + 1) * b:(i + 2) * b] = a_hi
                left_all[:, (i + 2) * b:(i + 3) * b] = a_lo
        for target in range(WIDTH):
            rows = right_all.at[target % 2]
            for j, inner in enumerate(range(target - REACH, REACH + 1)):
                if target >= inner:
                    m = block_source(k, inner, target - inner, *right)
                else:
                    m = block_source(k, target, inner - target, *right).T
                m_hi, m_lo = split(m)
                rows[3 * j * b:(3 * j + 1) * b, :] = m_hi
                rows[(3 * j + 1) * b:(3 * j + 2) * b, :] = m_lo
                rows[(3 * j + 2) * b:(3 * j + 3) * b, :] = m_hi
            depth = 3 * (2 * REACH + 1 - target) * b
            total = jnp.dot(
                left_all[:, 3 * target * b:],
                rows[:depth, :],
                preferred_element_type=jnp.float32,
            )
            total = flags[target] * total
            if final:
                total = 3.0 * right_in[0][target] - 2.0 * total
            out[target] = total

    for k in (0, 1):
        pl.when(parity[0] == k)(lambda k=k: compute(k))


def band_call(parity, flags, arrays, final):
    vmem = pl.BlockSpec(memory_space=pltpu.VMEM)
    smem = pl.BlockSpec(memory_space=pltpu.SMEM)
    local = arrays[-4]
    b = local.shape[-1]
    depth = 3 * (2 * REACH + 1) * b
    square_shape = jax.ShapeDtypeStruct(local.shape, jnp.float32)
    left_shape = jax.ShapeDtypeStruct((b, depth), jnp.bfloat16)
    return pl.pallas_call(
        functools.partial(band_kernel, final=final),
        out_shape=square_shape if final else (square_shape, left_shape),
        in_specs=[smem, smem] + [vmem] * len(arrays),
        out_specs=vmem if final else (vmem, vmem),
        scratch_shapes=[pltpu.VMEM((2, depth, b), jnp.bfloat16)],
        interpret=INTERPRET,
    )(parity, flags, *arrays)


def exchange_rows(x, is_odd, n):
    partner = swap_in_chip(jnp.where(is_odd, x[: WIDTH - 1], x[1:]), n)
    received = []
    for d in range(1, CHIPS_OUT + 1):
        up = jnp.concatenate([x[2 * d - 1:], partner[2 * d - 1:]], axis=0)
        down = jnp.concatenate([x[: 8 - 2 * d], partner[: 7 - 2 * d]], axis=0)
        buf = jnp.where(is_odd, up, down)
        step = 2 * d - 1
        route = [(i, (i + step) % n) if i % 2 else (i, (i - step) % n) for i in range(n)]
        received.append(lax.ppermute(buf, AXES, route))
    got = jnp.concatenate(received, axis=0)

    def kept(sender):
        return jnp.concatenate([got[a:b] for a, b in KEPT[sender]], axis=0)

    other = swap_in_chip(jnp.where(is_odd, kept(1), kept(0)), n)
    return (x, partner, got, other)


def on_device(density, pattern):
    local_band = density[0]
    n = lax.axis_size("row") * lax.axis_size("col")
    position = lax.axis_index("row") * lax.axis_size("col") + lax.axis_index("col")
    is_odd = (position % 2) == 1
    parity = (position % 2).astype(jnp.int32).reshape(1)
    columns = (position + jnp.arange(WIDTH, dtype=jnp.int32)) % n
    flags = jnp.any(pattern[0][None, :] == columns[:, None], axis=1).astype(jnp.float32)
    chip_p = exchange_rows(local_band, is_odd, n)
    square, left_all = band_call(parity, flags, chip_p, final=False)
    chip_s = exchange_rows(square, is_odd, n)
    purified = band_call(parity, flags, (left_all,) + chip_s, final=True)
    return purified[None]


def solution(mesh):
    return jax.shard_map(
        on_device,
        mesh=mesh,
        in_specs=(P(AXES, None, None, None), P(AXES, None)),
        out_specs=P(AXES, None, None, None),
        check_vma=False,
    )
```
